1024 devices in a mesh: ctx: 128 (over z, y), head: 8 (over x, core).
Axes of the slice: x: 4, y: 4, z: 32, core: 2. Of those that a mesh axis runs over, the one named last changes fastest.
Arguments:
- queries: bfloat16 [32768, 4096], P('ctx', 'head'), may hold values from -6 to 6
- key_rows: bfloat16 [32768, 4096], P('ctx', 'head'), may hold values from -1.5 to 1.5
- value_rows: bfloat16 [32768, 4096], P('ctx', 'head'), may hold values from -6 to 6
- carry_state: float32 [32, 128, 128], P('head'), may hold values from -96 to 96
- decay_rate: float32 [32], P('head'), as said below
- norm_gain: float32 [4096], P('head'), may hold values from 0.5 to 1.5
- order: int32 [128, 256], P('ctx'), may hold values from 0 to 255, each once within a row
- doc_lengths: int32 [256], replicated, may hold values from 1 to 2048, 32768 in all
Outputs:
- mixed: bfloat16 [32768, 4096], P('ctx', 'head')
The draws below stay inside these ranges and needn't reach their ends.
Inputs may be any that keep to these rules, and one draw needn't show every extreme that they name: `order`: each row is a permutation of 0..255. `doc_lengths`: they sum to 32768; the longest is exactly 2048. `decay_rate`: positive rates.
All inputs are finite; a program needn't handle non-finite values.
Results may differ from the reference program's by a relative error of at most 0.001.
Values may be sent and summed in bfloat16 or wider, within the bound.
No kernel may reach another device: no remote copies, remote signals or barrier semaphores. Data moves between devices by JAX's collectives and lax.ppermute only.
A program may use at most 128 MiB of HBM per device.

```python
import math
import jax
import jax.numpy as jnp
import numpy as np
from jax import lax

TOK_DEV = 256
DH = 128
HEADS = 32
TOKENS = 32768
SPILL = 64
BLOCK = 256
DOC_MOST = 2048
NDOCS = 256
N_CTX = 128


def draw_decay_rate(key, part):
    pick_key, fast_key, slow_key = jax.random.split(jax.random.fold_in(key, 7), 3)
    fast_share = 0.5
    is_fast = jax.random.uniform(pick_key, (HEADS,), jnp.float32) < fast_share
    fast_rate = jnp.exp(jax.random.uniform(fast_key, (HEADS,), jnp.float32, jnp.log(1.0 / 50.0), jnp.log(1.0 / 30.0)))
    slow_rate = jnp.exp(jax.random.uniform(slow_key, (HEADS,), jnp.float32, jnp.log(0.05), jnp.log(2.0))) / DOC_MOST
    return jnp.where(is_fast, fast_rate, slow_rate).astype(jnp.float32)


def steps_of(rng, extent, cuts, smallest, high):
    loudness = 1.0
    for dim, blocks in cuts:
        heights = jax.random.uniform(jax.random.fold_in(jax.random.fold_in(rng, 6), dim), (blocks,), jnp.float32, smallest / len(cuts), high / len(cuts))
        loudness = loudness * jnp.repeat(jnp.exp(heights), extent[dim] // blocks).reshape((-1,) + (1,) * (len(extent) - 1 - dim))
    return loudness


def length_profile(amount, total, most, lean):
    portions = [(1 << 20) // math.isqrt(standing ** lean) + 1 for standing in range(2, amount + 1)]
    surplus, given = total - most - (amount - 1), [1] * (amount - 1)
    while surplus > 0:
        movable = [i for i in range(amount - 1) if given[i] < most]
        pool, remaining = sum([portions[i] for i in movable]), surplus
        for i in movable:
            extra = min(most - given[i], max(1, remaining * portions[i] // pool), surplus)
            given[i] = given[i] + extra
            surplus = surplus - extra
    return np.array([most] + given)


def ragged(stream_key, count, total, bound, skew):
    if count == 2:
        one = jax.random.randint(stream_key, (), max(1, total - bound), min(bound, total - 1) + 1)
        return jnp.stack([one, total - one])
    sizes = jnp.asarray(length_profile(count, total, bound, skew), jnp.int32)
    couples = (count - 1) // 2
    donor, receiver = sizes[1:1 + 2 * couples:2], sizes[2:2 + 2 * couples:2]
    slack = jnp.minimum(donor - 1, bound - receiver)
    shifted = jax.random.randint(jax.random.fold_in(stream_key, 1), (couples,), 0, 1 << 20) % (slack + 1)
    sizes = sizes.at[1:1 + 2 * couples:2].set(donor - shifted).at[2:2 + 2 * couples:2].set(receiver + shifted)
    return sizes[jax.random.permutation(jax.random.fold_in(stream_key, 2), count)]


def centred(key, extent, scale, bound, cuts=(), held_as=jnp.bfloat16):
    level = steps_of(key, extent, cuts, -0.22, 0.18) if cuts else 1.0
    array = jax.random.normal(key, extent, jnp.float32) * scale * level
    return jnp.minimum(jnp.maximum(array, -bound), bound).astype(held_as)


def setup_inputs(seed: int = 0) -> dict:
    arg_keys = jax.random.split(jax.random.key(seed), 9)
    return {
        "queries": centred(arg_keys[0], (TOKENS, HEADS * DH), 1.0, 6.0, ((0, 128), (1, 8))),
        "key_rows": centred(arg_keys[1], (TOKENS, HEADS * DH), 0.25, 1.5, ((0, 128), (1, 8))),
        "value_rows": centred(arg_keys[2], (TOKENS, HEADS * DH), 1.0, 6.0, ((0, 128), (1, 8))),
        "carry_state": centred(arg_keys[3], (HEADS, DH, DH), 16.0, 96.0, ((0, 8),), jnp.float32),
        "decay_rate": draw_decay_rate(jax.random.fold_in(arg_keys[8], 71), 0),
        "norm_gain": jnp.clip(1.0 + 0.1 * jax.random.normal(arg_keys[5], (HEADS * DH,), jnp.float32), 0.5, 1.5),
        "order": jax.vmap(lambda own: jax.random.permutation(own, TOK_DEV))(jax.random.split(arg_keys[6], N_CTX)).reshape((N_CTX, TOK_DEV)).astype(jnp.int32),
        "doc_lengths": ragged(arg_keys[7], NDOCS, TOKENS, DOC_MOST, 2).astype(jnp.int32),
    }


def reference(queries, key_rows, value_rows, carry_state, decay_rate, norm_gain, order, doc_lengths):
    devices = jnp.arange(N_CTX, dtype=jnp.int32)[:, None]
    columns = jnp.arange(TOK_DEV, dtype=jnp.int32)[None, :]
    following = (devices + 1) % N_CTX
    source = jnp.where(columns < TOK_DEV - SPILL, devices * TOK_DEV + order, following * TOK_DEV + order[following[:, 0]])
    source = source.reshape(-1).astype(jnp.int32)
    doc_ends = jnp.cumsum(doc_lengths).astype(jnp.int32)
    positions = jnp.arange(TOKENS, dtype=jnp.int32)
    segment = jnp.searchsorted(doc_ends, positions, side='right').astype(jnp.int32)
    block_count = TOKENS // BLOCK
    starts = jnp.arange(block_count, dtype=jnp.int32) * BLOCK - 1
    previous = jnp.searchsorted(doc_ends, starts, side='right').astype(jnp.int32)
    shape = (block_count, BLOCK, HEADS, DH)
    ctx_query = queries[source].reshape(shape)
    ctx_key = key_rows[source].reshape(shape)
    ctx_value = value_rows[source].reshape(shape)
    segments = segment.reshape(block_count, BLOCK)
    rates = decay_rate.astype(jnp.float32)
    offsets = jnp.arange(BLOCK, dtype=jnp.int32)
    distance = offsets[:, None] - offsets[None, :]
    lower = distance >= 0
    decay = jnp.exp(-rates[:, None, None] * jnp.maximum(distance, 0).astype(jnp.float32)[None])
    leading = jnp.exp(-rates[None, :] * (offsets + 1).astype(jnp.float32)[:, None])
    trailing = jnp.exp(-rates[None, :] * (BLOCK - 1 - offsets).astype(jnp.float32)[:, None])
    whole_block = jnp.exp(-rates * jnp.float32(BLOCK))
    highest = lax.Precision.HIGHEST
    gains = norm_gain.astype(jnp.float32)

    def block_step(running, inputs):
        query_f, key_f, value_f, seg_ids, prior = inputs
        query_f = query_f.astype(jnp.float32)
        key_f = key_f.astype(jnp.float32)
        value_f = value_f.astype(jnp.float32)
        same_doc = (seg_ids[:, None] == seg_ids[None, :]) & lower
        scores = jnp.einsum('thd,shd->hts', query_f, key_f, precision=highest)
        weights = jnp.where(same_doc[None], scores * decay, jnp.float32(0.0))
        attn = jnp.einsum('hts,shd->thd', weights, value_f, precision=highest)
        carry_on = (seg_ids == prior).astype(jnp.float32)
        inter = jnp.einsum('thd,hde->the', query_f, running, precision=highest)
        attn = attn + inter * (leading * carry_on[:, None])[:, :, None]
        at_end = (seg_ids == seg_ids[-1]).astype(jnp.float32)
        added = jnp.einsum('shd,she->hde', key_f * (trailing * at_end[:, None])[:, :, None], value_f, precision=highest)
        keep_factor = jnp.where(seg_ids[-1] == prior, whole_block, jnp.float32(0.0))
        running = keep_factor[:, None, None] * running + added
        flat = attn.reshape(BLOCK, HEADS * DH)
        mean_sq = lax.optimization_barrier(jnp.mean(flat * flat, axis=1, keepdims=True))
        normed = (flat * lax.rsqrt(mean_sq + 1e-05) * gains[None, :]).astype(jnp.bfloat16)
        return (running, normed)
    _, outputs = lax.scan(block_step, carry_state.astype(jnp.float32), (ctx_query, ctx_key, ctx_value, segments, previous))
    result = jnp.zeros((TOKENS, HEADS * DH), jnp.bfloat16)
    return result.at[source].set(outputs.reshape(TOKENS, HEADS * DH))
```

```python
import jax
import jax.numpy as jnp
from jax import lax
from jax.sharding import PartitionSpec as P


def shifted(value, axis, steps, wrap_sources=()):
    count = lax.axis_size(axis)
    pairs = [(source, source + steps) for source in range(count - steps)]
    pairs += [(source, (source + steps) % count) for source in wrap_sources]
    return lax.ppermute(value, axis, pairs)


def shards(queries, key_rows, value_rows, carry_state, decay_rate, norm_gain, order, doc_lengths):
    row_count, feature_count = queries.shape
    head_count = decay_rate.shape[0]
    head_width = feature_count // head_count
    spill_count = row_count // 4
    kept_count = row_count - spill_count
    ctx_count = lax.axis_size("ctx")
    total = row_count * ctx_count
    highest = lax.Precision.HIGHEST
    device = lax.axis_index("ctx")
    rates = decay_rate.astype(jnp.float32)
    doc_ends = jnp.cumsum(doc_lengths)

    def doc_of(position):
        return jnp.sum((doc_ends[None, :] <= position[:, None]).astype(jnp.int32), axis=1)

    rows = jnp.arange(row_count, dtype=jnp.int32)
    slot_of_column = (rows + spill_count) % row_count
    window = jnp.sum(
        jnp.where(order[0][None, :] == rows[:, None], slot_of_column[None, :], 0), axis=1
    )
    position = (device * row_count - spill_count + window) % total
    segment = doc_of(position)

    def window_bounds(index):
        first = index == 0
        prior_pos = jnp.where(first, -1, index * row_count - spill_count - 1)
        end_pos = index * row_count + kept_count - 1
        prior_seg = doc_of(prior_pos)
        end_seg = doc_of(end_pos)
        span = jnp.where(first, kept_count, row_count).astype(jnp.float32)
        through = jnp.where(
            (prior_seg == end_seg)[:, None], jnp.exp(-rates[None, :] * span[:, None]), jnp.float32(0.0)
        )
        return end_seg, through

    near = (device - jnp.arange(5, dtype=jnp.int32)) % ctx_count
    end_segs, through = window_bounds(near)
    in_seg = doc_of(((device * row_count - spill_count - 1) % total)[None])[0]
    end_seg = end_segs[0]

    q = queries.reshape(row_count, head_count, head_width)
    k = key_rows.reshape(row_count, head_count, head_width)
    v = value_rows.reshape(row_count, head_count, head_width)
    q_f = q.astype(jnp.float32)
    k_f = k.astype(jnp.float32)
    v_f = v.astype(jnp.float32)

    at_end = segment == end_seg
    trailing = jnp.where(
        at_end[:, None],
        jnp.exp(-rates[None, :] * (row_count - 1 - window).astype(jnp.float32)[:, None]),
        jnp.float32(0.0),
    )
    running = jnp.einsum("shd,she->hde", k_f * trailing[:, :, None], v_f, precision=highest)
    initial = carry_state * (device == 0).astype(jnp.float32)
    element = through[0][:, None, None] * initial + running

    got = shifted(element, "ctx", 1)
    pair = through[0][:, None, None] * got + element
    got = shifted(pair, "ctx", 2)
    quad = (through[0] * through[1])[:, None, None] * got + pair
    near_quad = shifted(quad, "ctx", 1, wrap_sources=(ctx_count - 1,))
    far_quad = shifted(quad, "ctx", 5, wrap_sources=(ctx_count - 5,))
    span4 = through[1] * through[2] * through[3] * through[4]
    incoming = span4[:, None, None] * far_quad + near_quad

    distance = window[:, None] - window[None, :]
    same_doc = (segment[:, None] == segment[None, :]) & (distance >= 0)
    decay = jnp.exp(-rates[:, None, None] * jnp.maximum(distance, 0).astype(jnp.float32)[None])
    scores = jnp.einsum("thd,shd->hts", q, k, preferred_element_type=jnp.float32)
    weights = jnp.where(same_doc[None], scores * decay, jnp.float32(0.0))
    attn = jnp.einsum("hts,shd->thd", weights, v_f, precision=highest)

    lead_in = jnp.where(
        (segment == in_seg)[:, None],
        jnp.exp(-rates[None, :] * (window + 1).astype(jnp.float32)[:, None]),
        jnp.float32(0.0),
    )
    lead_init = jnp.where(
        ((segment == 0) & (device == 0))[:, None],
        jnp.exp(-rates[None, :] * (window - spill_count + 1).astype(jnp.float32)[:, None]),
        jnp.float32(0.0),
    )
    carried = jnp.einsum("thd,hde->the", q_f, incoming, precision=highest)
    started = jnp.einsum("thd,hde->the", q_f, initial, precision=highest)
    attn = attn + carried * lead_in[:, :, None] + started * lead_init[:, :, None]

    flat = attn.reshape(row_count, feature_count)
    square_total = lax.psum(jnp.sum(flat * flat, axis=1), "head")
    mean_sq = square_total / jnp.float32(feature_count * lax.axis_size("head"))
    return (flat * lax.rsqrt(mean_sq + 1e-05)[:, None] * norm_gain[None, :]).astype(jnp.bfloat16)


def solution(mesh):
    return jax.shard_map(
        shards,
        mesh=mesh,
        in_specs=(
            P("ctx", "head"),
            P("ctx", "head"),
            P("ctx", "head"),
            P("head", None, None),
            P("head"),
            P("head"),
            P("ctx", None),
            P(),
        ),
        out_specs=P("ctx", "head"),
        check_vma=False,
    )
```

```python
import jax
import jax.numpy as jnp
from jax import lax
from jax.sharding import PartitionSpec as P


def shifted(value, axis, steps, wrap_sources=()):
    count = lax.axis_size(axis)
    pairs = [(source, source + steps) for source in range(count - steps)]
    pairs += [(source, (source + steps) % count) for source in wrap_sources]
    return lax.ppermute(value, axis, pairs)


def shards(queries, key_rows, value_rows, carry_state, decay_rate, norm_gain, order, doc_lengths):
    row_count, feature_count = queries.shape
    head_count = decay_rate.shape[0]
    head_width = feature_count // head_count
    spill_count = row_count // 4
    kept_count = row_count - spill_count
    ctx_count = lax.axis_size("ctx")
    total = row_count * ctx_count
    highest = lax.Precision.HIGHEST
    device = lax.axis_index("ctx")
    rates = decay_rate.astype(jnp.float32)
    doc_ends = jnp.cumsum(doc_lengths)

    def doc_of(position):
        return jnp.sum((doc_ends[None, :] <= position[:, None]).astype(jnp.int32), axis=1)

    rows = jnp.arange(row_count, dtype=jnp.int32)
    slot_of_column = (rows + spill_count) % row_count
    window = jnp.sum(
        jnp.where(order[0][None, :] == rows[:, None], slot_of_column[None, :], 0), axis=1
    )
    position = (device * row_count - spill_count + window) % total
    segment = doc_of(position)

    def window_bounds(index):
        first = index == 0
        prior_pos = jnp.where(first, -1, index * row_count - spill_count - 1)
        end_pos = index * row_count + kept_count - 1
        prior_seg = doc_of(prior_pos)
        end_seg = doc_of(end_pos)
        span = jnp.where(first, kept_count, row_count).astype(jnp.float32)
        through = jnp.where(
            (prior_seg == end_seg)[:, None], jnp.exp(-rates[None, :] * span[:, None]), jnp.float32(0.0)
        )
        return end_seg, through

    near = (device - jnp.arange(5, dtype=jnp.int32)) % ctx_count
    end_segs, through = window_bounds(near)
    in_seg = doc_of(((device * row_count - spill_count - 1) % total)[None])[0]
    end_seg = end_segs[0]

    q = queries.reshape(row_count, head_count, head_width)
    k = key_rows.reshape(row_count, head_count, head_width)
    v = value_rows.reshape(row_count, head_count, head_width)
    q_f = q.astype(jnp.float32)
    k_f = k.astype(jnp.float32)
    v_f = v.astype(jnp.float32)

    at_end = segment == end_seg
    trailing = jnp.where(
        at_end[:, None],
        jnp.exp(-rates[None, :] * (row_count - 1 - window).astype(jnp.float32)[:, None]),
        jnp.float32(0.0),
    )
    running = jnp.einsum("shd,she->hde", k_f * trailing[:, :, None], v_f, precision=highest)
    initial = carry_state * (device == 0).astype(jnp.float32)
    element = through[0][:, None, None] * initial + running

    last = ctx_count - 1
    e1 = shifted(element, "ctx", 1, wrap_sources=(last,))
    e2 = shifted(element, "ctx", 2, wrap_sources=(last - 1,))
    e3 = shifted(element, "ctx", 3, wrap_sources=(last - 2,))
    e4 = shifted(element, "ctx", 4)
    t0, t1, t2, t3 = (through[i][:, None, None] for i in range(4))
    inner = (device != 0).astype(jnp.float32)
    reach1 = t0 * inner
    reach2 = reach1 * t1
    reach3 = reach2 * t2
    five = element + reach1 * e1 + reach2 * e2 + reach3 * e3 + reach3 * t3 * e4
    three = e1 + t1 * e2 + t1 * t2 * e3
    far = shifted(five, "ctx", 4, wrap_sources=(last - 3,))
    incoming = three + t1 * t2 * t3 * far

    distance = window[:, None] - window[None, :]
    same_doc = (segment[:, None] == segment[None, :]) & (distance >= 0)
    decay = jnp.exp(-rates[:, None, None] * jnp.maximum(distance, 0).astype(jnp.float32)[None])
    scores = jnp.einsum("thd,shd->hts", q, k, preferred_element_type=jnp.float32)
    weights = jnp.where(same_doc[None], scores * decay, jnp.float32(0.0))
    attn = jnp.einsum("hts,shd->thd", weights, v_f, precision=highest)

    lead_in = jnp.where(
        (segment == in_seg)[:, None],
        jnp.exp(-rates[None, :] * (window + 1).astype(jnp.float32)[:, None]),
        jnp.float32(0.0),
    )
    lead_init = jnp.where(
        ((segment == 0) & (device == 0))[:, None],
        jnp.exp(-rates[None, :] * (window - spill_count + 1).astype(jnp.float32)[:, None]),
        jnp.float32(0.0),
    )
    carried = jnp.einsum("thd,hde->the", q_f, incoming, precision=highest)
    started = jnp.einsum("thd,hde->the", q_f, initial, precision=highest)
    attn = attn + carried * lead_in[:, :, None] + started * lead_init[:, :, None]

    flat = attn.reshape(row_count, feature_count)
    square_total = lax.psum(jnp.sum(flat * flat, axis=1), "head")
    mean_sq = square_total / jnp.float32(feature_count * lax.axis_size("head"))
    return (flat * lax.rsqrt(mean_sq + 1e-05)[:, None] * norm_gain[None, :]).astype(jnp.bfloat16)


def solution(mesh):
    return jax.shard_map(
        shards,
        mesh=mesh,
        in_specs=(
            P("ctx", "head"),
            P("ctx", "head"),
            P("ctx", "head"),
            P("head", None, None),
            P("head"),
            P("head"),
            P("ctx", None),
            P(),
        ),
        out_specs=P("ctx", "head"),
        check_vma=False,
    )
```

```python
import jax
import jax.numpy as jnp
from jax import lax
from jax.sharding import PartitionSpec as P


def shifted(value, axis, steps, wrap_sources=()):
    count = lax.axis_size(axis)
    pairs = [(source, source + steps) for source in range(count - steps)]
    pairs += [(source, (source + steps) % count) for source in wrap_sources]
    return lax.ppermute(value, axis, pairs)


def shards(queries, key_rows, value_rows, carry_state, decay_rate, norm_gain, order, doc_lengths):
    row_count, feature_count = queries.shape
    head_count = decay_rate.shape[0]
    head_width = feature_count // head_count
    spill_count = row_count // 4
    kept_count = row_count - spill_count
    ctx_count = lax.axis_size("ctx")
    total = row_count * ctx_count
    highest = lax.Precision.HIGHEST
    device = lax.axis_index("ctx")
    rates = decay_rate.astype(jnp.float32)
    doc_ends = jnp.cumsum(doc_lengths)

    def doc_of(position):
        return jnp.sum((doc_ends[None, :] <= position[:, None]).astype(jnp.int32), axis=1)

    rows = jnp.arange(row_count, dtype=jnp.int32)
    slot_of_column = (rows + spill_count) % row_count
    window = jnp.sum(
        jnp.where(order[0][None, :] == rows[:, None], slot_of_column[None, :], 0), axis=1
    )
    position = (device * row_count - spill_count + window) % total
    segment = doc_of(position)

    def window_bounds(index):
        first = index == 0
        prior_pos = jnp.where(first, -1, index * row_count - spill_count - 1)
        end_pos = index * row_count + kept_count - 1
        prior_seg = doc_of(prior_pos)
        end_seg = doc_of(end_pos)
        span = jnp.where(first, kept_count, row_count).astype(jnp.float32)
        through = jnp.where(
            (prior_seg == end_seg)[:, None], jnp.exp(-rates[None, :] * span[:, None]), jnp.float32(0.0)
        )
        return end_seg, through

    near = (device - jnp.arange(5, dtype=jnp.int32)) % ctx_count
    end_segs, through = window_bounds(near)
    in_seg = doc_of(((device * row_count - spill_count - 1) % total)[None])[0]
    end_seg = end_segs[0]

    q = queries.reshape(row_count, head_count, head_width)
    k = key_rows.reshape(row_count, head_count, head_width)
    v = value_rows.reshape(row_count, head_count, head_width)
    q_f = q.astype(jnp.float32)
    k_f = k.astype(jnp.float32)
    v_f = v.astype(jnp.float32)

    at_end = segment == end_seg
    trailing = jnp.where(
        at_end[:, None],
        jnp.exp(-rates[None, :] * (row_count - 1 - window).astype(jnp.float32)[:, None]),
        jnp.float32(0.0),
    )
    running = jnp.einsum("shd,she->hde", k_f * trailing[:, :, None], v_f, precision=highest)
    initial = carry_state * (device == 0).astype(jnp.float32)
    element = through[0][:, None, None] * initial + running

    last = ctx_count - 1
    e1 = shifted(element, "ctx", 1, wrap_sources=(last,))
    e2 = shifted(element, "ctx", 2, wrap_sources=(last - 1,))
    e3 = shifted(element, "ctx", 3, wrap_sources=(last - 2,))
    e4 = shifted(element, "ctx", 4)
    t0, t1, t2, t3 = (through[i][:, None, None] for i in range(4))
    inner = (device != 0).astype(jnp.float32)
    reach1 = t0 * inner
    reach2 = reach1 * t1
    reach3 = reach2 * t2
    five = element + reach1 * e1 + reach2 * e2 + reach3 * e3 + reach3 * t3 * e4
    three = e1 + t1 * e2 + t1 * t2 * e3
    far = shifted(five, "ctx", 4, wrap_sources=(last - 3,))
    incoming = three + t1 * t2 * t3 * far

    distance = window[:, None] - window[None, :]
    same_doc = (segment[:, None] == segment[None, :]) & (distance >= 0)
    decay = jnp.exp(-rates[:, None, None] * jnp.maximum(distance, 0).astype(jnp.float32)[None])
    scores = jnp.einsum("thd,shd->hts", q, k, preferred_element_type=jnp.float32)
    weights = jnp.where(same_doc[None], scores * decay, jnp.float32(0.0))
    attn = jnp.einsum("hts,shd->thd", weights, v_f, precision=highest)

    lead_in = jnp.where(
        (segment == in_seg)[:, None],
        jnp.exp(-rates[None, :] * (window + 1).astype(jnp.float32)[:, None]),
        jnp.float32(0.0),
    )
    lead_init = jnp.where(
        ((segment == 0) & (device == 0))[:, None],
        jnp.exp(-rates[None, :] * (window - spill_count + 1).astype(jnp.float32)[:, None]),
        jnp.float32(0.0),
    )
    carried = jnp.einsum("thd,hde->the", q_f, incoming, precision=highest)
    started = jnp.einsum("thd,hde->the", q_f, initial, precision=highest)
    attn = attn + carried * lead_in[:, :, None] + started * lead_init[:, :, None]

    flat = attn.reshape(row_count, feature_count)
    square_total = lax.psum(lax.psum(jnp.sum(flat * flat, axis=1), "core"), "chip")
    mean_sq = square_total / jnp.float32(feature_count * lax.axis_size("chip") * lax.axis_size("core"))
    return (flat * lax.rsqrt(mean_sq + 1e-05)[:, None] * norm_gain[None, :]).astype(jnp.bfloat16)


def solution(mesh):
    split = jax.sharding.Mesh(
        mesh.devices.reshape(mesh.shape["ctx"], mesh.shape["head"] // 2, 2), ("ctx", "chip", "core")
    )
    head = ("chip", "core")
    return jax.shard_map(
        shards,
        mesh=split,
        in_specs=(
            P("ctx", head),
            P("ctx", head),
            P("ctx", head),
            P(head, None, None),
            P(head),
            P(head),
            P("ctx", None),
            P(),
        ),
        out_specs=P("ctx", head),
        check_vma=False,
    )
```

```python
import jax
import jax.numpy as jnp
from jax import lax
from jax.sharding import PartitionSpec as P


def shifted(value, axis, steps, wrap_sources=()):
    count = lax.axis_size(axis)
    pairs = [(source, source + steps) for source in range(count - steps)]
    pairs += [(source, (source + steps) % count) for source in wrap_sources]
    return lax.ppermute(value, axis, pairs)


def shards(queries, key_rows, value_rows, carry_state, decay_rate, norm_gain, order, doc_lengths):
    row_count, feature_count = queries.shape
    head_count = decay_rate.shape[0]
    head_width = feature_count // head_count
    spill_count = row_count // 4
    kept_count = row_count - spill_count
    ctx_count = lax.axis_size("ctx")
    total = row_count * ctx_count
    highest = lax.Precision.HIGHEST
    device = lax.axis_index("ctx")
    rates = decay_rate.astype(jnp.float32)
    doc_ends = jnp.cumsum(doc_lengths)

    def doc_of(position):
        return jnp.sum((doc_ends[None, :] <= position[:, None]).astype(jnp.int32), axis=1)

    rows = jnp.arange(row_count, dtype=jnp.int32)
    slot_of_column = (rows + spill_count) % row_count
    window = jnp.sum(
        jnp.where(order[0][None, :] == rows[:, None], slot_of_column[None, :], 0), axis=1
    )
    position = (device * row_count - spill_count + window) % total
    segment = doc_of(position)

    def window_bounds(index):
        first = index == 0
        prior_pos = jnp.where(first, -1, index * row_count - spill_count - 1)
        end_pos = index * row_count + kept_count - 1
        prior_seg = doc_of(prior_pos)
        end_seg = doc_of(end_pos)
        span = jnp.where(first, kept_count, row_count).astype(jnp.float32)
        through = jnp.where(
            (prior_seg == end_seg)[:, None], jnp.exp(-rates[None, :] * span[:, None]), jnp.float32(0.0)
        )
        return end_seg, through

    near = (device - jnp.arange(6, dtype=jnp.int32)) % ctx_count
    end_segs, through = window_bounds(near)
    in_seg = doc_of(((device * row_count - spill_count - 1) % total)[None])[0]
    end_seg = end_segs[0]

    q = queries.reshape(row_count, head_count, head_width)
    k = key_rows.reshape(row_count, head_count, head_width)
    v = value_rows.reshape(row_count, head_count, head_width)
    q_f = q.astype(jnp.float32)
    k_f = k.astype(jnp.float32)
    v_f = v.astype(jnp.float32)

    at_end = segment == end_seg
    trailing = jnp.where(
        at_end[:, None],
        jnp.exp(-rates[None, :] * (row_count - 1 - window).astype(jnp.float32)[:, None]),
        jnp.float32(0.0),
    )
    running = jnp.einsum("shd,she->hde", k_f * trailing[:, :, None], v_f, precision=highest)
    initial = carry_state * (device == 0).astype(jnp.float32)
    element = through[0][:, None, None] * initial + running

    last = ctx_count - 1
    e1 = shifted(element, "ctx", 1, wrap_sources=(last,))
    e2 = shifted(element, "ctx", 2, wrap_sources=(last - 1,))
    t0, t1, t2, t3, t4, t5 = (through[i][:, None, None] for i in range(6))
    reach1 = t0 * (device != 0).astype(jnp.float32)
    three = element + reach1 * e1 + reach1 * t1 * e2
    two = e1 + t1 * e2
    mid = shifted(three, "ctx", 3, wrap_sources=(last - 2,))
    far = shifted(three, "ctx", 6, wrap_sources=(last - 5,))
    span2 = t1 * t2
    incoming = two + span2 * mid + span2 * t3 * t4 * t5 * far

    distance = window[:, None] - window[None, :]
    same_doc = (segment[:, None] == segment[None, :]) & (distance >= 0)
    decay = jnp.exp(-rates[:, None, None] * jnp.maximum(distance, 0).astype(jnp.float32)[None])
    scores = jnp.einsum("thd,shd->hts", q, k, preferred_element_type=jnp.float32)
    weights = jnp.where(same_doc[None], scores * decay, jnp.float32(0.0))
    attn = jnp.einsum("hts,shd->thd", weights, v_f, precision=highest)

    lead_in = jnp.where(
        (segment == in_seg)[:, None],
        jnp.exp(-rates[None, :] * (window + 1).astype(jnp.float32)[:, None]),
        jnp.float32(0.0),
    )
    lead_init = jnp.where(
        ((segment == 0) & (device == 0))[:, None],
        jnp.exp(-rates[None, :] * (window - spill_count + 1).astype(jnp.float32)[:, None]),
        jnp.float32(0.0),
    )
    carried = jnp.einsum("thd,hde->the", q_f, incoming, precision=highest)
    started = jnp.einsum("thd,hde->the", q_f, initial, precision=highest)
    attn = attn + carried * lead_in[:, :, None] + started * lead_init[:, :, None]

    flat = attn.reshape(row_count, feature_count)
    square_total = lax.psum(lax.psum(jnp.sum(flat * flat, axis=1), "core"), "chip")
    mean_sq = square_total / jnp.float32(feature_count * lax.axis_size("chip") * lax.axis_size("core"))
    return (flat * lax.rsqrt(mean_sq + 1e-05)[:, None] * norm_gain[None, :]).astype(jnp.bfloat16)


def solution(mesh):
    split = jax.sharding.Mesh(
        mesh.devices.reshape(mesh.shape["ctx"], mesh.shape["head"] // 2, 2), ("ctx", "chip", "core")
    )
    head = ("chip", "core")
    return jax.shard_map(
        shards,
        mesh=split,
        in_specs=(
            P("ctx", head),
            P("ctx", head),
            P("ctx", head),
            P(head, None, None),
            P(head),
            P(head),
            P("ctx", None),
            P(),
        ),
        out_specs=P("ctx", head),
        check_vma=False,
    )
```

```python
import jax
import jax.numpy as jnp
from jax import lax
from jax.sharding import PartitionSpec as P


def shifted(value, axis, steps, wrap_sources=()):
    count = lax.axis_size(axis)
    pairs = [(source, source + steps) for source in range(count - steps)]
    pairs += [(source, (source + steps) % count) for source in wrap_sources]
    return lax.ppermute(value, axis, pairs)


def shards(queries, key_rows, value_rows, carry_state, decay_rate, norm_gain, order, doc_lengths):
    row_count, feature_count = queries.shape
    head_count = decay_rate.shape[0]
    head_width = feature_count // head_count
    spill_count = row_count // 4
    kept_count = row_count - spill_count
    ctx_count = lax.axis_size("ctx")
    total = row_count * ctx_count
    highest = lax.Precision.HIGHEST
    device = lax.axis_index("ctx")
    rates = decay_rate.astype(jnp.float32)
    doc_ends = jnp.cumsum(doc_lengths)

    def doc_of(position):
        return jnp.sum((doc_ends[None, :] <= position[:, None]).astype(jnp.int32), axis=1)

    rows = jnp.arange(row_count, dtype=jnp.int32)
    slot_of_column = (rows + spill_count) % row_count
    window = jnp.sum(
        jnp.where(order[0][None, :] == rows[:, None], slot_of_column[None, :], 0), axis=1
    )
    position = (device * row_count - spill_count + window) % total
    segment = doc_of(position)

    def window_bounds(index):
        first = index == 0
        prior_pos = jnp.where(first, -1, index * row_count - spill_count - 1)
        end_pos = index * row_count + kept_count - 1
        prior_seg = doc_of(prior_pos)
        end_seg = doc_of(end_pos)
        span = jnp.where(first, kept_count, row_count).astype(jnp.float32)
        through = jnp.where(
            (prior_seg == end_seg)[:, None], jnp.exp(-rates[None, :] * span[:, None]), jnp.float32(0.0)
        )
        return end_seg, through

    near = (device - jnp.arange(6, dtype=jnp.int32)) % ctx_count
    end_segs, through = window_bounds(near)
    in_seg = doc_of(((device * row_count - spill_count - 1) % total)[None])[0]
    end_seg = end_segs[0]

    q = queries.reshape(row_count, head_count, head_width)
    k = key_rows.reshape(row_count, head_count, head_width)
    v = value_rows.reshape(row_count, head_count, head_width)
    q_f = q.astype(jnp.float32)
    k_f = k.astype(jnp.float32)
    v_f = v.astype(jnp.float32)

    at_end = segment == end_seg
    trailing = jnp.where(
        at_end[:, None],
        jnp.exp(-rates[None, :] * (row_count - 1 - window).astype(jnp.float32)[:, None]),
        jnp.float32(0.0),
    )
    running = jnp.einsum("shd,she->hde", k_f * trailing[:, :, None], v_f, precision=highest)
    initial = carry_state * (device == 0).astype(jnp.float32)
    element = through[0][:, None, None] * initial + running

    last = ctx_count - 1
    e1 = shifted(element, "ctx", 1, wrap_sources=(last,))
    e2 = shifted(element, "ctx", 2, wrap_sources=(last - 1,))
    t0, t1, t2, t3, t4, t5 = (through[i][:, None, None] for i in range(6))
    reach1 = t0 * (device != 0).astype(jnp.float32)
    three = element + reach1 * e1 + reach1 * t1 * e2
    two = e1 + t1 * e2
    mid = shifted(three, "ctx", 3, wrap_sources=(last - 2,))
    far = shifted(three, "ctx", 6, wrap_sources=(last - 5,))
    span2 = t1 * t2
    incoming = two + span2 * mid + span2 * t3 * t4 * t5 * far

    distance = window[:, None] - window[None, :]
    same_doc = (segment[:, None] == segment[None, :]) & (distance >= 0)
    decay = jnp.exp(-rates[:, None, None] * jnp.maximum(distance, 0).astype(jnp.float32)[None])
    scores = jnp.einsum("thd,shd->hts", q, k, preferred_element_type=jnp.float32)
    weights = jnp.where(same_doc[None], scores * decay, jnp.float32(0.0))
    attn = jnp.einsum("hts,shd->thd", weights, v_f, precision=highest)

    lead_in = jnp.where(
        (segment == in_seg)[:, None],
        jnp.exp(-rates[None, :] * (window + 1).astype(jnp.float32)[:, None]),
        jnp.float32(0.0),
    )
    lead_init = jnp.where(
        ((segment == 0) & (device == 0))[:, None],
        jnp.exp(-rates[None, :] * (window - spill_count + 1).astype(jnp.float32)[:, None]),
        jnp.float32(0.0),
    )
    carried = jnp.einsum("thd,hde->the", q_f, incoming, precision=highest)
    started = jnp.einsum("thd,hde->the", q_f, initial, precision=highest)
    attn = attn + carried * lead_in[:, :, None] + started * lead_init[:, :, None]

    flat = attn.reshape(row_count, feature_count)
    on_chip = lax.psum(jnp.sum(flat * flat, axis=1), "core")
    chips = lax.axis_size("chip")
    square_total = on_chip
    for step in range(1, chips):
        square_total = square_total + lax.ppermute(
            on_chip, "chip", [(source, (source + step) % chips) for source in range(chips)]
        )
    mean_sq = square_total / jnp.float32(feature_count * lax.axis_size("chip") * lax.axis_size("core"))
    return (flat * lax.rsqrt(mean_sq + 1e-05)[:, None] * norm_gain[None, :]).astype(jnp.bfloat16)


def solution(mesh):
    split = jax.sharding.Mesh(
        mesh.devices.reshape(mesh.shape["ctx"], mesh.shape["head"] // 2, 2), ("ctx", "chip", "core")
    )
    head = ("chip", "core")
    return jax.shard_map(
        shards,
        mesh=split,
        in_specs=(
            P("ctx", head),
            P("ctx", head),
            P("ctx", head),
            P(head, None, None),
            P(head),
            P(head),
            P("ctx", None),
            P(),
        ),
        out_specs=P("ctx", head),
        check_vma=False,
    )
```

```python
import jax
import jax.numpy as jnp
from jax import lax
from jax.sharding import PartitionSpec as P


def shifted(value, axis, steps, wrap_sources=()):
    count = lax.axis_size(axis)
    pairs = [(source, source + steps) for source in range(count - steps)]
    pairs += [(source, (source + steps) % count) for source in wrap_sources]
    return lax.ppermute(value, axis, pairs)


def shards(queries, key_rows, value_rows, carry_state, decay_rate, norm_gain, order, doc_lengths):
    row_count, feature_count = queries.shape
    head_count = decay_rate.shape[0]
    head_width = feature_count // head_count
    spill_count = row_count // 4
    kept_count = row_count - spill_count
    ctx_count = lax.axis_size("ctx")
    total = row_count * ctx_count
    highest = lax.Precision.HIGHEST
    device = lax.axis_index("ctx")
    rates = decay_rate.astype(jnp.float32)
    doc_ends = jnp.cumsum(doc_lengths)

    def doc_of(position):
        return jnp.sum((doc_ends[None, :] <= position[:, None]).astype(jnp.int32), axis=1)

    rows = jnp.arange(row_count, dtype=jnp.int32)
    slot_of_column = (rows + spill_count) % row_count
    window = jnp.sum(
        jnp.where(order[0][None, :] == rows[:, None], slot_of_column[None, :], 0), axis=1
    )
    position = (device * row_count - spill_count + window) % total
    segment = doc_of(position)

    def window_bounds(index):
        first = index == 0
        prior_pos = jnp.where(first, -1, index * row_count - spill_count - 1)
        end_pos = index * row_count + kept_count - 1
        prior_seg = doc_of(prior_pos)
        end_seg = doc_of(end_pos)
        span = jnp.where(first, kept_count, row_count).astype(jnp.float32)
        through = jnp.where(
            (prior_seg == end_seg)[:, None], jnp.exp(-rates[None, :] * span[:, None]), jnp.float32(0.0)
        )
        return end_seg, through

    near = (device - jnp.arange(6, dtype=jnp.int32)) % ctx_count
    end_segs, through = window_bounds(near)
    in_seg = doc_of(((device * row_count - spill_count - 1) % total)[None])[0]
    end_seg = end_segs[0]

    q = queries.reshape(row_count, head_count, head_width)
    k = key_rows.reshape(row_count, head_count, head_width)
    v = value_rows.reshape(row_count, head_count, head_width)
    q_f = q.astype(jnp.float32)
    k_f = k.astype(jnp.float32)
    v_f = v.astype(jnp.float32)

    at_end = segment == end_seg
    trailing = jnp.where(
        at_end[:, None],
        jnp.exp(-rates[None, :] * (row_count - 1 - window).astype(jnp.float32)[:, None]),
        jnp.float32(0.0),
    )
    running = jnp.einsum("shd,she->hde", k_f * trailing[:, :, None], v_f, precision=highest)
    initial = carry_state * (device == 0).astype(jnp.float32)
    element = through[0][:, None, None] * initial + running

    last = ctx_count - 1
    e1 = shifted(element, "ctx", 1, wrap_sources=(last,))
    e2 = shifted(element, "ctx", 2, wrap_sources=(last - 1,))
    t0, t1, t2, t3, t4, t5 = (through[i][:, None, None] for i in range(6))
    reach1 = t0 * (device != 0).astype(jnp.float32)
    three = element + reach1 * e1 + reach1 * t1 * e2
    two = e1 + t1 * e2
    mid = shifted(three, "ctx", 3, wrap_sources=(last - 2,))
    far = shifted(three, "ctx", 6, wrap_sources=(last - 5,))
    span2 = t1 * t2
    incoming = two + span2 * mid + span2 * t3 * t4 * t5 * far

    distance = window[:, None] - window[None, :]
    same_doc = (segment[:, None] == segment[None, :]) & (distance >= 0)
    decay = jnp.exp(-rates[:, None, None] * jnp.maximum(distance, 0).astype(jnp.float32)[None])
    scores = jnp.einsum("thd,shd->hts", q, k, preferred_element_type=jnp.float32)
    weights = jnp.where(same_doc[None], scores * decay, jnp.float32(0.0))
    attn = jnp.einsum("hts,shd->thd", weights, v_f, precision=highest)

    lead_in = jnp.where(
        (segment == in_seg)[:, None],
        jnp.exp(-rates[None, :] * (window + 1).astype(jnp.float32)[:, None]),
        jnp.float32(0.0),
    )
    lead_init = jnp.where(
        ((segment == 0) & (device == 0))[:, None],
        jnp.exp(-rates[None, :] * (window - spill_count + 1).astype(jnp.float32)[:, None]),
        jnp.float32(0.0),
    )
    carried = jnp.einsum("thd,hde->the", q_f, incoming, precision=highest)
    started = jnp.einsum("thd,hde->the", q_f, initial, precision=highest)
    attn = attn + carried * lead_in[:, :, None] + started * lead_init[:, :, None]

    flat = attn.reshape(row_count, feature_count)
    groups = lax.axis_size("chip") * lax.axis_size("core")
    part = jnp.broadcast_to(jnp.sum(flat * flat, axis=1)[None], (groups, row_count))
    square_total = jnp.sum(lax.all_to_all(part, ("chip", "core"), 0, 0), axis=0)
    mean_sq = square_total / jnp.float32(feature_count * lax.axis_size("chip") * lax.axis_size("core"))
    return (flat * lax.rsqrt(mean_sq + 1e-05)[:, None] * norm_gain[None, :]).astype(jnp.bfloat16)


def solution(mesh):
    split = jax.sharding.Mesh(
        mesh.devices.reshape(mesh.shape["ctx"], mesh.shape["head"] // 2, 2), ("ctx", "chip", "core")
    )
    head = ("chip", "core")
    return jax.shard_map(
        shards,
        mesh=split,
        in_specs=(
            P("ctx", head),
            P("ctx", head),
            P("ctx", head),
            P(head, None, None),
            P(head),
            P(head),
            P("ctx", None),
            P(),
        ),
        out_specs=P("ctx", head),
        check_vma=False,
    )
```

```python
import jax
import jax.numpy as jnp
from jax import lax
from jax.sharding import PartitionSpec as P


def shifted(value, axis, steps, wrap_sources=()):
    count = lax.axis_size(axis)
    pairs = [(source, source + steps) for source in range(count - steps)]
    pairs += [(source, (source + steps) % count) for source in wrap_sources]
    return lax.ppermute(value, axis, pairs)


def shards(queries, key_rows, value_rows, carry_state, decay_rate, norm_gain, order, doc_lengths):
    row_count, feature_count = queries.shape
    head_count = decay_rate.shape[0]
    head_width = feature_count // head_count
    spill_count = row_count // 4
    kept_count = row_count - spill_count
    ctx_count = lax.axis_size("ctx")
    total = row_count * ctx_count
    highest = lax.Precision.HIGHEST
    device = lax.axis_index("ctx")
    rates = decay_rate.astype(jnp.float32)
    doc_ends = jnp.cumsum(doc_lengths)

    def doc_of(position):
        return jnp.sum((doc_ends[None, :] <= position[:, None]).astype(jnp.int32), axis=1)

    rows = jnp.arange(row_count, dtype=jnp.int32)
    slot_of_column = (rows + spill_count) % row_count
    window = jnp.sum(
        jnp.where(order[0][None, :] == rows[:, None], slot_of_column[None, :], 0), axis=1
    )
    position = (device * row_count - spill_count + window) % total
    segment = doc_of(position)

    def window_bounds(index):
        first = index == 0
        prior_pos = jnp.where(first, -1, index * row_count - spill_count - 1)
        end_pos = index * row_count + kept_count - 1
        prior_seg = doc_of(prior_pos)
        end_seg = doc_of(end_pos)
        span = jnp.where(first, kept_count, row_count).astype(jnp.float32)
        through = jnp.where(
            (prior_seg == end_seg)[:, None], jnp.exp(-rates[None, :] * span[:, None]), jnp.float32(0.0)
        )
        return end_seg, through

    near = (device - jnp.arange(5, dtype=jnp.int32)) % ctx_count
    end_segs, through = window_bounds(near)
    in_seg = doc_of(((device * row_count - spill_count - 1) % total)[None])[0]
    end_seg = end_segs[0]

    q = queries.reshape(row_count, head_count, head_width)
    k = key_rows.reshape(row_count, head_count, head_width)
    v = value_rows.reshape(row_count, head_count, head_width)
    q_f = q.astype(jnp.float32)
    k_f = k.astype(jnp.float32)
    v_f = v.astype(jnp.float32)

    at_end = segment == end_seg
    trailing = jnp.where(
        at_end[:, None],
        jnp.exp(-rates[None, :] * (row_count - 1 - window).astype(jnp.float32)[:, None]),
        jnp.float32(0.0),
    )
    running = jnp.einsum("shd,she->hde", k_f * trailing[:, :, None], v_f, precision=highest)
    initial = carry_state * (device == 0).astype(jnp.float32)
    element = through[0][:, None, None] * initial + running

    last = ctx_count - 1
    e1 = shifted(element, "ctx", 1, wrap_sources=(last,))
    e2 = shifted(element, "ctx", 2, wrap_sources=(last - 1,))
    e3 = shifted(element, "ctx", 3, wrap_sources=(last - 2,))
    e4 = shifted(element, "ctx", 4)
    t0, t1, t2, t3 = (through[i][:, None, None] for i in range(4))
    inner = (device != 0).astype(jnp.float32)
    reach1 = t0 * inner
    reach2 = reach1 * t1
    reach3 = reach2 * t2
    five = element + reach1 * e1 + reach2 * e2 + reach3 * e3 + reach3 * t3 * e4
    three = e1 + t1 * e2 + t1 * t2 * e3
    far = shifted(five, "ctx", 4, wrap_sources=(last - 3,))
    incoming = three + t1 * t2 * t3 * far

    distance = window[:, None] - window[None, :]
    same_doc = (segment[:, None] == segment[None, :]) & (distance >= 0)
    decay = jnp.exp(-rates[:, None, None] * jnp.maximum(distance, 0).astype(jnp.float32)[None])
    scores = jnp.einsum("thd,shd->hts", q, k, preferred_element_type=jnp.float32)
    weights = jnp.where(same_doc[None], scores * decay, jnp.float32(0.0))
    attn = jnp.einsum("hts,shd->thd", weights, v_f, precision=highest)

    lead_in = jnp.where(
        (segment == in_seg)[:, None],
        jnp.exp(-rates[None, :] * (window + 1).astype(jnp.float32)[:, None]),
        jnp.float32(0.0),
    )
    lead_init = jnp.where(
        ((segment == 0) & (device == 0))[:, None],
        jnp.exp(-rates[None, :] * (window - spill_count + 1).astype(jnp.float32)[:, None]),
        jnp.float32(0.0),
    )
    carried = jnp.einsum("thd,hde->the", q_f, incoming, precision=highest)
    started = jnp.einsum("thd,hde->the", q_f, initial, precision=highest)
    attn = attn + carried * lead_in[:, :, None] + started * lead_init[:, :, None]

    flat = attn.reshape(row_count, feature_count)
    groups = lax.axis_size("chip") * lax.axis_size("core")
    part = jnp.broadcast_to(jnp.sum(flat * flat, axis=1)[None], (groups, row_count))
    square_total = jnp.sum(lax.all_to_all(part, ("chip", "core"), 0, 0), axis=0)
    mean_sq = square_total / jnp.float32(feature_count * lax.axis_size("chip") * lax.axis_size("core"))
    return (flat * lax.rsqrt(mean_sq + 1e-05)[:, None] * norm_gain[None, :]).astype(jnp.bfloat16)


def solution(mesh):
    split = jax.sharding.Mesh(
        mesh.devices.reshape(mesh.shape["ctx"], mesh.shape["head"] // 2, 2), ("ctx", "chip", "core")
    )
    head = ("chip", "core")
    return jax.shard_map(
        shards,
        mesh=split,
        in_specs=(
            P("ctx", head),
            P("ctx", head),
            P("ctx", head),
            P(head, None, None),
            P(head),
            P(head),
            P("ctx", None),
            P(),
        ),
        out_specs=P("ctx", head),
        check_vma=False,
    )
```

```python
import jax
import jax.numpy as jnp
from jax import lax
from jax.sharding import PartitionSpec as P


def shifted(value, axis, steps, wrap_sources=()):
    count = lax.axis_size(axis)
    pairs = [(source, source + steps) for source in range(count - steps)]
    pairs += [(source, (source + steps) % count) for source in wrap_sources]
    return lax.ppermute(value, axis, pairs)


def shards(queries, key_rows, value_rows, carry_state, decay_rate, norm_gain, order, doc_lengths):
    row_count, feature_count = queries.shape
    head_count = decay_rate.shape[0]
    head_width = feature_count // head_count
    spill_count = row_count // 4
    kept_count = row_count - spill_count
    ctx_count = lax.axis_size("ctx")
    total = row_count * ctx_count
    highest = lax.Precision.HIGHEST
    device = lax.axis_index("ctx")
    rates = decay_rate.astype(jnp.float32)
    doc_ends = jnp.cumsum(doc_lengths)

    def doc_of(position):
        return jnp.sum((doc_ends[None, :] <= position[:, None]).astype(jnp.int32), axis=1)

    rows = jnp.arange(row_count, dtype=jnp.int32)
    slot_of_column = (rows + spill_count) % row_count
    window = jnp.sum(
        jnp.where(order[0][None, :] == rows[:, None], slot_of_column[None, :], 0), axis=1
    )
    position = (device * row_count - spill_count + window) % total
    segment = doc_of(position)

    def window_bounds(index):
        first = index == 0
        prior_pos = jnp.where(first, -1, index * row_count - spill_count - 1)
        end_pos = index * row_count + kept_count - 1
        prior_seg = doc_of(prior_pos)
        end_seg = doc_of(end_pos)
        span = jnp.where(first, kept_count, row_count).astype(jnp.float32)
        through = jnp.where(
            (prior_seg == end_seg)[:, None], jnp.exp(-rates[None, :] * span[:, None]), jnp.float32(0.0)
        )
        return end_seg, through

    near = (device - jnp.arange(5, dtype=jnp.int32)) % ctx_count
    end_segs, through = window_bounds(near)
    in_seg = doc_of(((device * row_count - spill_count - 1) % total)[None])[0]
    end_seg = end_segs[0]

    q = queries.reshape(row_count, head_count, head_width)
    k = key_rows.reshape(row_count, head_count, head_width)
    v = value_rows.reshape(row_count, head_count, head_width)
    q_f = q.astype(jnp.float32)
    k_f = k.astype(jnp.float32)
    v_f = v.astype(jnp.float32)

    at_end = segment == end_seg
    trailing = jnp.where(
        at_end[:, None],
        jnp.exp(-rates[None, :] * (row_count - 1 - window).astype(jnp.float32)[:, None]),
        jnp.float32(0.0),
    )
    running = jnp.einsum("shd,she->hde", k_f * trailing[:, :, None], v_f, precision=highest)
    initial = carry_state * (device == 0).astype(jnp.float32)
    element = through[0][:, None, None] * initial + running

    last = ctx_count - 1
    e1 = shifted(element, "ctx", 1, wrap_sources=(last,))
    e2 = shifted(element, "ctx", 2, wrap_sources=(last - 1,))
    e3 = shifted(element, "ctx", 3, wrap_sources=(last - 2,))
    e4 = shifted(element, "ctx", 4)
    t0, t1, t2, t3 = (through[i][:, None, None] for i in range(4))
    inner = (device != 0).astype(jnp.float32)
    reach1 = t0 * inner
    reach2 = reach1 * t1
    reach3 = reach2 * t2
    five = element + reach1 * e1 + reach2 * e2 + reach3 * e3 + reach3 * t3 * e4
    three = e1 + t1 * e2 + t1 * t2 * e3
    far = shifted(five, "ctx", 4, wrap_sources=(last - 3,))
    incoming = three + t1 * t2 * t3 * far

    distance = window[:, None] - window[None, :]
    same_doc = (segment[:, None] == segment[None, :]) & (distance >= 0)
    decay = jnp.exp(-rates[:, None, None] * jnp.maximum(distance, 0).astype(jnp.float32)[None])
    scores = jnp.einsum("thd,shd->hts", q, k, preferred_element_type=jnp.float32)
    weights = jnp.where(same_doc[None], scores * decay, jnp.float32(0.0))
    attn = jnp.einsum("hts,shd->thd", weights, v_f, precision=highest)
    attn, gain_rows = lax.optimization_barrier(
        (attn, jnp.broadcast_to(norm_gain[None, :], (row_count, feature_count)))
    )

    lead_in = jnp.where(
        (segment == in_seg)[:, None],
        jnp.exp(-rates[None, :] * (window + 1).astype(jnp.float32)[:, None]),
        jnp.float32(0.0),
    )
    lead_init = jnp.where(
        ((segment == 0) & (device == 0))[:, None],
        jnp.exp(-rates[None, :] * (window - spill_count + 1).astype(jnp.float32)[:, None]),
        jnp.float32(0.0),
    )
    carried = jnp.einsum("thd,hde->the", q_f, incoming, precision=highest)
    started = jnp.einsum("thd,hde->the", q_f, initial, precision=highest)
    attn = attn + carried * lead_in[:, :, None] + started * lead_init[:, :, None]

    flat = attn.reshape(row_count, feature_count)
    groups = lax.axis_size("chip") * lax.axis_size("core")
    part = jnp.broadcast_to(jnp.sum(flat * flat, axis=1)[None], (groups, row_count))
    square_total = jnp.sum(lax.all_to_all(part, ("chip", "core"), 0, 0), axis=0)
    mean_sq = square_total / jnp.float32(feature_count * lax.axis_size("chip") * lax.axis_size("core"))
    return (flat * lax.rsqrt(mean_sq + 1e-05)[:, None] * gain_rows).astype(jnp.bfloat16)


def solution(mesh):
    split = jax.sharding.Mesh(
        mesh.devices.reshape(mesh.shape["ctx"], mesh.shape["head"] // 2, 2), ("ctx", "chip", "core")
    )
    head = ("chip", "core")
    return jax.shard_map(
        shards,
        mesh=split,
        in_specs=(
            P("ctx", head),
            P("ctx", head),
            P("ctx", head),
            P(head, None, None),
            P(head),
            P(head),
            P("ctx", None),
            P(),
        ),
        out_specs=P("ctx", head),
        check_vma=False,
    )
```

```python
import jax
import jax.numpy as jnp
from jax import lax
from jax.sharding import PartitionSpec as P


def shifted(value, axis, steps, wrap_sources=()):
    count = lax.axis_size(axis)
    pairs = [(source, source + steps) for source in range(count - steps)]
    pairs += [(source, (source + steps) % count) for source in wrap_sources]
    return lax.ppermute(value, axis, pairs)


def shards(queries, key_rows, value_rows, carry_state, decay_rate, norm_gain, order, doc_lengths):
    row_count, feature_count = queries.shape
    head_count = decay_rate.shape[0]
    head_width = feature_count // head_count
    spill_count = row_count // 4
    kept_count = row_count - spill_count
    ctx_count = lax.axis_size("ctx")
    total = row_count * ctx_count
    highest = lax.Precision.HIGHEST
    device = lax.axis_index("ctx")
    rates = decay_rate.astype(jnp.float32)
    doc_ends = jnp.cumsum(doc_lengths)

    def doc_of(position):
        return jnp.sum((doc_ends[None, :] <= position[:, None]).astype(jnp.int32), axis=1)

    rows = jnp.arange(row_count, dtype=jnp.int32)
    slot_of_column = (rows + spill_count) % row_count
    window = jnp.sum(
        jnp.where(order[0][None, :] == rows[:, None], slot_of_column[None, :], 0), axis=1
    )
    position = (device * row_count - spill_count + window) % total
    segment = doc_of(position)

    def window_bounds(index):
        first = index == 0
        prior_pos = jnp.where(first, -1, index * row_count - spill_count - 1)
        end_pos = index * row_count + kept_count - 1
        prior_seg = doc_of(prior_pos)
        end_seg = doc_of(end_pos)
        span = jnp.where(first, kept_count, row_count).astype(jnp.float32)
        through = jnp.where(
            (prior_seg == end_seg)[:, None], jnp.exp(-rates[None, :] * span[:, None]), jnp.float32(0.0)
        )
        return end_seg, through

    near = (device - jnp.arange(6, dtype=jnp.int32)) % ctx_count
    end_segs, through = window_bounds(near)
    in_seg = doc_of(((device * row_count - spill_count - 1) % total)[None])[0]
    end_seg = end_segs[0]

    q = queries.reshape(row_count, head_count, head_width)
    k = key_rows.reshape(row_count, head_count, head_width)
    v = value_rows.reshape(row_count, head_count, head_width)
    q_f = q.astype(jnp.float32)
    k_f = k.astype(jnp.float32)
    v_f = v.astype(jnp.float32)

    at_end = segment == end_seg
    trailing = jnp.where(
        at_end[:, None],
        jnp.exp(-rates[None, :] * (row_count - 1 - window).astype(jnp.float32)[:, None]),
        jnp.float32(0.0),
    )
    running = jnp.einsum("shd,she->hde", k_f * trailing[:, :, None], v_f, precision=highest)
    initial = carry_state * (device == 0).astype(jnp.float32)
    element = through[0][:, None, None] * initial + running

    e1 = shifted(element, "ctx", 1)
    e2 = shifted(element, "ctx", 2)
    e3 = shifted(element, "ctx", 3)
    e4 = shifted(element, "ctx", 4)
    t0, t1, t2, t3, t4, t5 = (through[i][:, None, None] for i in range(6))
    reach2 = t0 * t1
    upto3 = element + t0 * e1 + reach2 * e2
    five = upto3 + reach2 * t2 * e3 + reach2 * t2 * t3 * e4
    three = e1 + t1 * e2 + t1 * t2 * e3
    last = ctx_count - 1
    far = lax.ppermute(five, "ctx", [(s, s + 4) for s in range(ctx_count - 4)] + [(last, 0)])
    tail = lax.ppermute(upto3, "ctx", [(last - 5, 0)])
    first = (device == 0).astype(jnp.float32)
    far_weight = first + (1.0 - first) * (t1 * t2 * t3)
    incoming = three + far_weight * far + first * (t1 * t2 * t3 * t4 * t5) * tail

    distance = window[:, None] - window[None, :]
    same_doc = (segment[:, None] == segment[None, :]) & (distance >= 0)
    decay = jnp.exp(-rates[:, None, None] * jnp.maximum(distance, 0).astype(jnp.float32)[None])
    scores = jnp.einsum("thd,shd->hts", q, k, preferred_element_type=jnp.float32)
    weights = jnp.where(same_doc[None], scores * decay, jnp.float32(0.0))
    attn = jnp.einsum("hts,shd->thd", weights, v_f, precision=highest)

    lead_in = jnp.where(
        (segment == in_seg)[:, None],
        jnp.exp(-rates[None, :] * (window + 1).astype(jnp.float32)[:, None]),
        jnp.float32(0.0),
    )
    lead_init = jnp.where(
        ((segment == 0) & (device == 0))[:, None],
        jnp.exp(-rates[None, :] * (window - spill_count + 1).astype(jnp.float32)[:, None]),
        jnp.float32(0.0),
    )
    carried = jnp.einsum("thd,hde->the", q_f, incoming, precision=highest)
    started = jnp.einsum("thd,hde->the", q_f, initial, precision=highest)
    attn = attn + carried * lead_in[:, :, None] + started * lead_init[:, :, None]

    flat = attn.reshape(row_count, feature_count)
    groups = lax.axis_size("chip") * lax.axis_size("core")
    part = jnp.broadcast_to(jnp.sum(flat * flat, axis=1)[None], (groups, row_count))
    square_total = jnp.sum(lax.all_to_all(part, ("chip", "core"), 0, 0), axis=0)
    mean_sq = square_total / jnp.float32(feature_count * lax.axis_size("chip") * lax.axis_size("core"))
    return (flat * lax.rsqrt(mean_sq + 1e-05)[:, None] * norm_gain[None, :]).astype(jnp.bfloat16)


def solution(mesh):
    split = jax.sharding.Mesh(
        mesh.devices.reshape(mesh.shape["ctx"], mesh.shape["head"] // 2, 2), ("ctx", "chip", "core")
    )
    head = ("chip", "core")
    return jax.shard_map(
        shards,
        mesh=split,
        in_specs=(
            P("ctx", head),
            P("ctx", head),
            P("ctx", head),
            P(head, None, None),
            P(head),
            P(head),
            P("ctx", None),
            P(),
        ),
        out_specs=P("ctx", head),
        check_vma=False,
    )
```

```python
import jax
import jax.numpy as jnp
from jax import lax
from jax.sharding import PartitionSpec as P


def shifted(value, axis, steps, wrap_sources=()):
    count = lax.axis_size(axis)
    pairs = [(source, source + steps) for source in range(count - steps)]
    pairs += [(source, (source + steps) % count) for source in wrap_sources]
    return lax.ppermute(value, axis, pairs)


def shards(queries, key_rows, value_rows, carry_state, decay_rate, norm_gain, order, doc_lengths):
    row_count, feature_count = queries.shape
    head_count = decay_rate.shape[0]
    head_width = feature_count // head_count
    spill_count = row_count // 4
    kept_count = row_count - spill_count
    ctx_count = lax.axis_size("ctx")
    total = row_count * ctx_count
    highest = lax.Precision.HIGHEST
    device = lax.axis_index("ctx")
    rates = decay_rate.astype(jnp.float32)
    doc_ends = jnp.cumsum(doc_lengths)

    def doc_of(position):
        return jnp.sum((doc_ends[None, :] <= position[:, None]).astype(jnp.int32), axis=1)

    rows = jnp.arange(row_count, dtype=jnp.int32)
    slot_of_column = (rows + spill_count) % row_count
    window = jnp.sum(
        jnp.where(order[0][None, :] == rows[:, None], slot_of_column[None, :], 0), axis=1
    )
    position = (device * row_count - spill_count + window) % total
    segment = doc_of(position)

    def window_bounds(index):
        first = index == 0
        prior_pos = jnp.where(first, -1, index * row_count - spill_count - 1)
        end_pos = index * row_count + kept_count - 1
        prior_seg = doc_of(prior_pos)
        end_seg = doc_of(end_pos)
        span = jnp.where(first, kept_count, row_count).astype(jnp.float32)
        through = jnp.where(
            (prior_seg == end_seg)[:, None], jnp.exp(-rates[None, :] * span[:, None]), jnp.float32(0.0)
        )
        return end_seg, through

    near = (device - jnp.arange(4, dtype=jnp.int32)) % ctx_count
    end_segs, through = window_bounds(near)
    in_seg = doc_of(((device * row_count - spill_count - 1) % total)[None])[0]
    end_seg = end_segs[0]

    q = queries.reshape(row_count, head_count, head_width)
    k = key_rows.reshape(row_count, head_count, head_width)
    v = value_rows.reshape(row_count, head_count, head_width)
    q_f = q.astype(jnp.float32)
    k_f = k.astype(jnp.float32)
    v_f = v.astype(jnp.float32)

    at_end = segment == end_seg
    trailing = jnp.where(
        at_end[:, None],
        jnp.exp(-rates[None, :] * (row_count - 1 - window).astype(jnp.float32)[:, None]),
        jnp.float32(0.0),
    )
    running = jnp.einsum("shd,she->hde", k_f * trailing[:, :, None], v_f, precision=highest)
    initial = carry_state * (device == 0).astype(jnp.float32)
    element = through[0][:, None, None] * initial + running

    e1 = shifted(element, "ctx", 1)
    e2 = shifted(element, "ctx", 2)
    e3 = shifted(element, "ctx", 3)
    e4 = shifted(element, "ctx", 4)
    t0, t1, t2, t3 = (through[i][:, None, None] for i in range(4))
    reach2 = t0 * t1
    upto3 = element + t0 * e1 + reach2 * e2
    five = upto3 + reach2 * t2 * e3 + reach2 * t2 * t3 * e4
    three = e1 + t1 * e2 + t1 * t2 * e3
    last = ctx_count - 1
    far = lax.ppermute(five, "ctx", [(s, s + 4) for s in range(ctx_count - 4)] + [(last - 3, 0)])
    tail = lax.ppermute(upto3, "ctx", [(last, 0)])
    incoming = three + t1 * t2 * t3 * far + tail

    distance = window[:, None] - window[None, :]
    same_doc = (segment[:, None] == segment[None, :]) & (distance >= 0)
    decay = jnp.exp(-rates[:, None, None] * jnp.maximum(distance, 0).astype(jnp.float32)[None])
    scores = jnp.einsum("thd,shd->hts", q, k, preferred_element_type=jnp.float32)
    weights = jnp.where(same_doc[None], scores * decay, jnp.float32(0.0))
    attn = jnp.einsum("hts,shd->thd", weights, v_f, precision=highest)

    lead_in = jnp.where(
        (segment == in_seg)[:, None],
        jnp.exp(-rates[None, :] * (window + 1).astype(jnp.float32)[:, None]),
        jnp.float32(0.0),
    )
    lead_init = jnp.where(
        ((segment == 0) & (device == 0))[:, None],
        jnp.exp(-rates[None, :] * (window - spill_count + 1).astype(jnp.float32)[:, None]),
        jnp.float32(0.0),
    )
    carried = jnp.einsum("thd,hde->the", q_f, incoming, precision=highest)
    started = jnp.einsum("thd,hde->the", q_f, initial, precision=highest)
    attn = attn + carried * lead_in[:, :, None] + started * lead_init[:, :, None]

    flat = attn.reshape(row_count, feature_count)
    groups = lax.axis_size("chip") * lax.axis_size("core")
    part = jnp.broadcast_to(jnp.sum(flat * flat, axis=1)[None], (groups, row_count))
    square_total = jnp.sum(lax.all_to_all(part, ("chip", "core"), 0, 0), axis=0)
    mean_sq = square_total / jnp.float32(feature_count * lax.axis_size("chip") * lax.axis_size("core"))
    return (flat * lax.rsqrt(mean_sq + 1e-05)[:, None] * norm_gain[None, :]).astype(jnp.bfloat16)


def solution(mesh):
    split = jax.sharding.Mesh(
        mesh.devices.reshape(mesh.shape["ctx"], mesh.shape["head"] // 2, 2), ("ctx", "chip", "core")
    )
    head = ("chip", "core")
    return jax.shard_map(
        shards,
        mesh=split,
        in_specs=(
            P("ctx", head),
            P("ctx", head),
            P("ctx", head),
            P(head, None, None),
            P(head),
            P(head),
            P("ctx", None),
            P(),
        ),
        out_specs=P("ctx", head),
        check_vma=False,
    )
```

```python
import jax
import jax.numpy as jnp
from jax import lax
from jax.sharding import PartitionSpec as P


def shifted(value, axis, steps, wrap_sources=()):
    count = lax.axis_size(axis)
    pairs = [(source, source + steps) for source in range(count - steps)]
    pairs += [(source, (source + steps) % count) for source in wrap_sources]
    return lax.ppermute(value, axis, pairs)


def shards(queries, key_rows, value_rows, carry_state, decay_rate, norm_gain, order, doc_lengths):
    row_count, feature_count = queries.shape
    head_count = decay_rate.shape[0]
    head_width = feature_count // head_count
    spill_count = row_count // 4
    kept_count = row_count - spill_count
    ctx_count = lax.axis_size("ctx")
    total = row_count * ctx_count
    highest = lax.Precision.HIGHEST
    device = lax.axis_index("ctx")
    rates = decay_rate.astype(jnp.float32)
    doc_ends = jnp.cumsum(doc_lengths)

    def doc_of(position):
        return jnp.sum((doc_ends[None, :] <= position[:, None]).astype(jnp.int32), axis=1)

    rows = jnp.arange(row_count, dtype=jnp.int32)
    slot_of_column = (rows + spill_count) % row_count
    window = jnp.sum(
        jnp.where(order[0][None, :] == rows[:, None], slot_of_column[None, :], 0), axis=1
    )
    position = (device * row_count - spill_count + window) % total
    segment = doc_of(position)

    def window_bounds(index):
        first = index == 0
        prior_pos = jnp.where(first, -1, index * row_count - spill_count - 1)
        end_pos = index * row_count + kept_count - 1
        prior_seg = doc_of(prior_pos)
        end_seg = doc_of(end_pos)
        span = jnp.where(first, kept_count, row_count).astype(jnp.float32)
        through = jnp.where(
            (prior_seg == end_seg)[:, None], jnp.exp(-rates[None, :] * span[:, None]), jnp.float32(0.0)
        )
        return end_seg, through

    near = (device - jnp.arange(6, dtype=jnp.int32)) % ctx_count
    end_segs, through = window_bounds(near)
    in_seg = doc_of(((device * row_count - spill_count - 1) % total)[None])[0]
    end_seg = end_segs[0]

    q = queries.reshape(row_count, head_count, head_width)
    k = key_rows.reshape(row_count, head_count, head_width)
    v = value_rows.reshape(row_count, head_count, head_width)
    q_f = q.astype(jnp.float32)
    k_f = k.astype(jnp.float32)
    v_f = v.astype(jnp.float32)

    at_end = segment == end_seg
    trailing = jnp.where(
        at_end[:, None],
        jnp.exp(-rates[None, :] * (row_count - 1 - window).astype(jnp.float32)[:, None]),
        jnp.float32(0.0),
    )
    running = jnp.einsum("shd,she->hde", k_f * trailing[:, :, None], v_f, precision=highest)
    initial = carry_state * (device == 0).astype(jnp.float32)
    element = through[0][:, None, None] * initial + running

    e1 = shifted(element, "ctx", 1)
    e2 = shifted(element, "ctx", 2)
    e3 = shifted(element, "ctx", 3)
    e4 = shifted(element, "ctx", 4)
    t0, t1, t2, t3, t4, t5 = (through[i][:, None, None] for i in range(6))
    reach2 = t0 * t1
    upto3 = element + t0 * e1 + reach2 * e2
    five = upto3 + reach2 * t2 * e3 + reach2 * t2 * t3 * e4
    three = e1 + t1 * e2 + t1 * t2 * e3
    last = ctx_count - 1
    far = lax.ppermute(five, "ctx", [(s, s + 4) for s in range(ctx_count - 4)] + [(last, 0)])
    tail = lax.ppermute(upto3, "ctx", [(last - 5, 0)])
    first = (device == 0).astype(jnp.float32)
    far_weight = first + (1.0 - first) * (t1 * t2 * t3)
    incoming = three + far_weight * far + first * (t1 * t2 * t3 * t4 * t5) * tail

    distance = window[:, None] - window[None, :]
    same_doc = (segment[:, None] == segment[None, :]) & (distance >= 0)
    decay = jnp.exp(-rates[:, None, None] * jnp.maximum(distance, 0).astype(jnp.float32)[None])
    scores = jnp.einsum("thd,shd->hts", q, k, preferred_element_type=jnp.float32)
    weights = jnp.where(same_doc[None], scores * decay, jnp.float32(0.0))
    attn = jnp.einsum("hts,shd->thd", weights, v_f, precision=highest)
    attn, gain_rows = lax.optimization_barrier(
        (attn, jnp.broadcast_to(norm_gain[None, :], (row_count, feature_count)))
    )

    lead_in = jnp.where(
        (segment == in_seg)[:, None],
        jnp.exp(-rates[None, :] * (window + 1).astype(jnp.float32)[:, None]),
        jnp.float32(0.0),
    )
    lead_init = jnp.where(
        ((segment == 0) & (device == 0))[:, None],
        jnp.exp(-rates[None, :] * (window - spill_count + 1).astype(jnp.float32)[:, None]),
        jnp.float32(0.0),
    )
    carried = jnp.einsum("thd,hde->the", q_f, incoming, precision=highest)
    started = jnp.einsum("thd,hde->the", q_f, initial, precision=highest)
    attn = attn + carried * lead_in[:, :, None] + started * lead_init[:, :, None]

    flat = attn.reshape(row_count, feature_count)
    groups = lax.axis_size("chip") * lax.axis_size("core")
    part = jnp.broadcast_to(jnp.sum(flat * flat, axis=1)[None], (groups, row_count))
    square_total = jnp.sum(lax.all_to_all(part, ("chip", "core"), 0, 0), axis=0)
    mean_sq = square_total / jnp.float32(feature_count * lax.axis_size("chip") * lax.axis_size("core"))
    return (flat * lax.rsqrt(mean_sq + 1e-05)[:, None] * gain_rows).astype(jnp.bfloat16)


def solution(mesh):
    split = jax.sharding.Mesh(
        mesh.devices.reshape(mesh.shape["ctx"], mesh.shape["head"] // 2, 2), ("ctx", "chip", "core")
    )
    head = ("chip", "core")
    return jax.shard_map(
        shards,
        mesh=split,
        in_specs=(
            P("ctx", head),
            P("ctx", head),
            P("ctx", head),
            P(head, None, None),
            P(head),
            P(head),
            P("ctx", None),
            P(),
        ),
        out_specs=P("ctx", head),
        check_vma=False,
    )
```
